512 devices in a mesh: expert: 64 (over x, z, core), group: 8 (over y).
Axes of the slice: x: 4, y: 8, z: 8, core: 2. Of those that a mesh axis runs over, the one named last changes fastest.
Arguments:
- tokens: bfloat16 [4096, 4096], P('expert', 'group'), may hold values from -6 to 6
- gate_weight: bfloat16 [64, 1536, 4096], P('expert', 'group'), may hold values from -0.09375 to 0.09375
- up_weight: bfloat16 [64, 1536, 4096], P('expert', 'group'), may hold values from -0.09375 to 0.09375
- down_weight: bfloat16 [64, 1536, 4096], P('expert', 'group'), may hold values from -0.15625 to 0.15625
- expert_ids: int32 [4096, 8], P('expert'), may hold values from 0 to 63, all different within a row; in each aligned block of 64 rows (0 to 63, 64 to 127, ...) at most 12 rows name the same one
- gate_scores: bfloat16 [4096, 8], P('expert'), may hold values from 0.19921875 to 1
Outputs:
- mixed: bfloat16 [4096, 4096], P('expert', 'group')
The draws below stay inside these ranges and needn't reach their ends.
Inputs may be any that keep to these rules, and one draw needn't show every extreme that they name: `expert_ids`: the 8 experts of a token are distinct; within the 64 rows of one device no expert is named by more than 12 rows, a bound that some block reaches.
All inputs are finite; a program needn't handle non-finite values.
Results may differ from the reference program's by a relative error of at most 0.019.
Values may be sent and summed in bfloat16 or wider, within the bound.
No kernel may reach another device: no remote copies, remote signals or barrier semaphores. Data moves between devices by JAX's collectives and lax.ppermute only.
A program may use at most 128 MiB of HBM per device.

```python
import math
import jax
import jax.numpy as jnp
import numpy as np
from jax import lax

D = 4096
FF = 1536
TOP = 8
TOK_IDX = 64
EXPERTS = 64
TOKENS = 4096
CAP = 12
N_EXPERT = 64
N_GROUP = 8


def block_scale(key, shape, split, least, largest):
    def one(axis_at, blocks):
        steps = jax.random.uniform(jax.random.fold_in(jax.random.fold_in(key, 6), axis_at), (blocks,), jnp.float32, least / len(split), largest / len(split))
        return jnp.repeat(jnp.exp(steps), shape[axis_at] // blocks).reshape((-1,) + (1,) * (len(shape) - axis_at - 1))

    gain = one(*split[0])
    for cut in split[1:]:
        gain = gain * one(*cut)
    return gain


def routed_block(stream_key, own, number, rows, count, top, bound, slope):
    order = jax.random.permutation(stream_key, count)
    packed, usual = portions_of(count, rows * top, bound, slope, True), portions_of(count, rows * top, bound, slope, False)
    places = jnp.arange(count)

    def named(lengths, turn):
        used = int((lengths > 0).sum())
        fixed = max(1, used // 4)
        passed = fixed + (places - fixed + turn * (used - fixed)) % max(1, count - fixed)
        return jnp.zeros((count,), jnp.int32).at[order[jnp.where(places < fixed, places, passed)]].set(jnp.asarray(lengths, jnp.int32))

    lengths = jnp.where(number % 4 == 0, named(packed, number // 4), named(usual, number - number // 4 - 1))
    mixed = jax.random.permutation(jax.random.fold_in(own, 3), count)
    source_of, sink = mixed[0:count // 2 * 2:2], mixed[1:count // 2 * 2:2]
    slack = jnp.minimum(lengths[source_of] - 1, bound - lengths[sink]) // 2
    slack = jnp.where((source_of == order[0]) | (sink == order[0]) | (lengths[sink] == 0), 0, jnp.maximum(slack, 0))
    passed = jax.random.randint(jax.random.fold_in(own, 4), (count // 2,), 0, 1 << 20) % (slack + 1)
    lengths = lengths.at[source_of].add(-passed).at[sink].add(passed)
    members = jnp.searchsorted(jnp.cumsum(lengths), jnp.arange(rows * top), side="right").astype(jnp.int32)
    grid = members.reshape(top, rows).T
    grid = grid[jax.random.permutation(jax.random.fold_in(own, 1), rows)]
    turn = jax.random.randint(jax.random.fold_in(own, 2), (rows, 1), 0, top)
    return jnp.take_along_axis(grid, (jnp.arange(top)[None, :] + turn) % top, axis=1)


def portions_of(count, total, limit, lean, full):
    loads = [(1 << 20) // math.isqrt(standing ** lean) + 1 for standing in range(1, count + 1)]
    largest = limit if full else min(limit, max(-(-total // count), total * loads[0] // sum(loads)))
    least = 1 if total - largest >= count - 1 else 0
    counts, rest = [largest] + [least] * (count - 1), total - largest - least * (count - 1)
    while rest > 0:
        candidates = [i for i in range(1, count) if counts[i] < largest] or [i for i in range(1, count) if counts[i] < limit]
        mass, budget = sum([loads[i] for i in candidates]), rest
        for i in candidates:
            addition = min(limit - counts[i], max(1, budget * loads[i] // mass), rest)
            counts[i] = counts[i] + addition
            rest = rest - addition
    return np.array(counts)


def gaussian(rng, dims, width, reach, pieces=(), kind=jnp.bfloat16):
    drawn = jax.random.normal(rng, dims, jnp.float32) * width
    if len(pieces) > 0:
        drawn = block_scale(rng, dims, pieces, -0.22, 0.18) * drawn
    return jnp.clip(drawn, min=-reach, max=reach).astype(kind)


def setup_inputs(seed: int = 0) -> dict:
    key_of = jax.random.split(jax.random.key(seed), 7)
    tokens = gaussian(key_of[0], (TOKENS, D), 1.0, 6.0, ((0, 64), (1, 8)))
    gate_weight = gaussian(key_of[1], (EXPERTS, FF, D), D ** -0.5, 0.09375, ((0, 64), (1, 8)))
    up_weight = gaussian(key_of[2], (EXPERTS, FF, D), D ** -0.5, 0.09375, ((0, 64), (1, 8)))
    down_weight = gaussian(key_of[3], (EXPERTS, FF, D), FF ** -0.5, 0.15625, ((0, 64), (1, 8)))
    expert_ids_keys = jax.random.split(jax.random.fold_in(key_of[4], 1), TOKENS // TOK_IDX)
    expert_ids_turns = jax.random.permutation(jax.random.fold_in(key_of[4], 3), TOKENS // TOK_IDX)
    expert_ids = jax.vmap(lambda own, number: routed_block(jax.random.fold_in(key_of[4], 2), own, number, TOK_IDX, EXPERTS, TOP, CAP, 2))(expert_ids_keys, expert_ids_turns).reshape((TOKENS, TOP))
    gate_scores = jnp.clip(0.19921875 + 0.80078125 * jax.random.uniform(key_of[5], (TOKENS, TOP), jnp.float32) ** block_scale(key_of[5], (TOKENS, TOP), ((0, 64),), -0.2, 0.2), 0.19921875, 1.0).astype(jnp.bfloat16)
    return {"tokens": tokens, "gate_weight": gate_weight, "up_weight": up_weight, "down_weight": down_weight, "expert_ids": expert_ids, "gate_scores": gate_scores}


def reference(tokens, gate_weight, up_weight, down_weight, expert_ids, gate_scores):
    blocks = N_EXPERT
    flat_ids = expert_ids.reshape(blocks, TOK_IDX * TOP)
    onehot = (flat_ids[:, :, None] == jnp.arange(EXPERTS, dtype=jnp.int32)[None, None, :]).astype(jnp.int32)
    before = jnp.cumsum(onehot, axis=1) - onehot
    slot_index = jnp.sum(before * onehot, axis=2).reshape(TOKENS, TOP).astype(jnp.int32)
    block_of = (jnp.arange(TOKENS, dtype=jnp.int32) // TOK_IDX).astype(jnp.int32)
    dest_index = ((expert_ids * blocks + block_of[:, None]) * CAP + slot_index).astype(jnp.int32)
    repeated = jnp.repeat(tokens, TOP, axis=0)
    routed = jnp.zeros((EXPERTS * blocks * CAP, D), jnp.bfloat16).at[dest_index.reshape(-1)].set(repeated)
    routed = routed.reshape(EXPERTS, blocks * CAP, D)
    slice_width = FF // N_GROUP

    def expert_out(operands):
        row_block, w_gate, w_up, w_down = operands
        gate_value = jnp.dot(row_block, w_gate.T, preferred_element_type=jnp.float32)
        up_value = jnp.dot(row_block, w_up.T, preferred_element_type=jnp.float32)
        hidden = (jax.nn.silu(gate_value) * up_value).astype(jnp.bfloat16)
        summed = jnp.zeros((row_block.shape[0], D), jnp.float32)
        for slice_num in range(N_GROUP):
            lower = slice_num * slice_width
            piece_out = jnp.dot(hidden[:, lower:lower + slice_width], w_down[lower:lower + slice_width], preferred_element_type=jnp.float32)
            summed = summed + lax.optimization_barrier(piece_out.astype(jnp.bfloat16)).astype(jnp.float32)
        return summed

    outputs = lax.map(expert_out, (routed, gate_weight, up_weight, down_weight))
    flat_out = outputs.reshape(EXPERTS * blocks * CAP, D)
    mixed = jnp.zeros((TOKENS, D), jnp.float32)
    for rank_k in range(TOP):
        mixed = mixed + gate_scores[:, rank_k:rank_k + 1].astype(jnp.float32) * flat_out[dest_index[:, rank_k]]
    return mixed.astype(jnp.bfloat16)
```

```python
import jax
import jax.numpy as jnp
from jax import lax
from jax.sharding import PartitionSpec as P


def route_tables(expert_ids, gate_scores, experts):
    tok_rows, top_count = expert_ids.shape
    capacity = tok_rows * top_count * 3 // (2 * experts)
    flat_ids = expert_ids.reshape(-1)
    onehot = (flat_ids[:, None] == jnp.arange(experts, dtype=jnp.int32)[None, :]).astype(jnp.int32)
    before = jnp.cumsum(onehot, axis=0) - onehot
    slot_index = jnp.sum(before * onehot, axis=1).reshape(tok_rows, top_count)
    slot_keys = expert_ids * capacity + slot_index
    columns = jnp.arange(experts * capacity, dtype=jnp.int32)
    matches = slot_keys[:, :, None] == columns[None, None, :]
    selector = jnp.any(matches, axis=1).astype(jnp.bfloat16)
    weights = jnp.sum(
        jnp.where(matches, gate_scores[:, :, None].astype(jnp.float32), 0.0), axis=1
    ).astype(jnp.bfloat16)
    return capacity, selector, weights


def per_device(tokens, gate_weight, up_weight, down_weight, expert_ids, gate_scores):
    experts = lax.axis_size("expert")
    capacity, selector, weights = route_tables(expert_ids, gate_scores, experts)
    placed = lax.dot_general(
        selector, tokens, (((0,), (0,)), ((), ())), preferred_element_type=jnp.float32
    ).astype(jnp.bfloat16)
    arrived = lax.all_to_all(
        placed.reshape(experts, capacity, tokens.shape[1]), "expert", 0, 0, tiled=True
    ).reshape(experts * capacity, tokens.shape[1])
    row_block = lax.all_gather(arrived, "group", axis=1, tiled=True)
    gate_value = lax.dot_general(
        row_block, gate_weight[0], (((1,), (1,)), ((), ())), preferred_element_type=jnp.float32
    )
    up_value = lax.dot_general(
        row_block, up_weight[0], (((1,), (1,)), ((), ())), preferred_element_type=jnp.float32
    )
    hidden = (jax.nn.silu(gate_value) * up_value).astype(jnp.bfloat16)
    partial_value = jnp.dot(hidden, down_weight[0], preferred_element_type=jnp.float32)
    summed = lax.psum_scatter(
        partial_value.astype(jnp.bfloat16), "group", scatter_dimension=1, tiled=True
    )
    returned = lax.all_to_all(
        summed.reshape(experts, capacity, summed.shape[1]), "expert", 0, 0, tiled=True
    ).reshape(experts * capacity, summed.shape[1])
    combined = jnp.dot(weights, returned, preferred_element_type=jnp.float32)
    return combined.astype(jnp.bfloat16)


def solution(mesh):
    placed = (
        P("expert", "group"),
        P("expert", "group", None),
        P("expert", "group", None),
        P("expert", "group", None),
        P("expert", None),
        P("expert", None),
    )
    return jax.shard_map(
        per_device, mesh=mesh, in_specs=placed, out_specs=P("expert", "group"), check_vma=False
    )
```

```python
import jax
import jax.numpy as jnp
from jax import lax
from jax.sharding import PartitionSpec as P

CHUNKS = 2


def route_tables(expert_ids, gate_scores, experts):
    tok_rows, top_count = expert_ids.shape
    capacity = tok_rows * top_count * 3 // (2 * experts)
    flat_ids = expert_ids.reshape(-1)
    onehot = (flat_ids[:, None] == jnp.arange(experts, dtype=jnp.int32)[None, :]).astype(jnp.int32)
    before = jnp.cumsum(onehot, axis=0) - onehot
    slot_index = jnp.sum(before * onehot, axis=1).reshape(tok_rows, top_count)
    slot_keys = expert_ids * capacity + slot_index
    columns = jnp.arange(experts * capacity, dtype=jnp.int32)
    matches = slot_keys[:, :, None] == columns[None, None, :]
    selector = jnp.any(matches, axis=1).astype(jnp.bfloat16)
    weights = jnp.sum(
        jnp.where(matches, gate_scores[:, :, None].astype(jnp.float32), 0.0), axis=1
    ).astype(jnp.bfloat16)
    return capacity, selector, weights


def expert_rows(chunk, gate_weight, up_weight, down_weight, experts, width):
    arrived = lax.all_to_all(
        chunk.reshape(experts, -1, width), "expert", 0, 0, tiled=True
    ).reshape(-1, width)
    row_block = lax.all_gather(arrived, "group", axis=1, tiled=True)
    gate_value = lax.dot_general(
        row_block, gate_weight[0], (((1,), (1,)), ((), ())), preferred_element_type=jnp.float32
    )
    up_value = lax.dot_general(
        row_block, up_weight[0], (((1,), (1,)), ((), ())), preferred_element_type=jnp.float32
    )
    hidden = (jax.nn.silu(gate_value) * up_value).astype(jnp.bfloat16)
    partial_value = jnp.dot(hidden, down_weight[0], preferred_element_type=jnp.float32)
    summed = lax.psum_scatter(
        partial_value.astype(jnp.bfloat16), "group", scatter_dimension=1, tiled=True
    )
    return lax.all_to_all(
        summed.reshape(experts, -1, width), "expert", 0, 0, tiled=True
    )


def per_device(tokens, gate_weight, up_weight, down_weight, expert_ids, gate_scores):
    experts = lax.axis_size("expert")
    width = tokens.shape[1]
    capacity, selector, weights = route_tables(expert_ids, gate_scores, experts)
    placed = lax.dot_general(
        selector, tokens, (((0,), (0,)), ((), ())), preferred_element_type=jnp.float32
    ).astype(jnp.bfloat16).reshape(experts, capacity, width)
    cut = capacity // CHUNKS
    pieces = []
    for c in range(CHUNKS):
        chunk = placed[:, c * cut:(c + 1) * cut]
        pieces.append(expert_rows(chunk, gate_weight, up_weight, down_weight, experts, width))
    returned = jnp.concatenate(pieces, axis=1).reshape(experts * capacity, width)
    combined = jnp.dot(weights, returned, preferred_element_type=jnp.float32)
    return combined.astype(jnp.bfloat16)


def solution(mesh):
    placed = (
        P("expert", "group"),
        P("expert", "group", None),
        P("expert", "group", None),
        P("expert", "group", None),
        P("expert", None),
        P("expert", None),
    )
    return jax.shard_map(
        per_device, mesh=mesh, in_specs=placed, out_specs=P("expert", "group"), check_vma=False
    )
```

```python
import jax
import jax.numpy as jnp
from jax import lax
from jax.sharding import PartitionSpec as P


def route_tables(expert_ids, gate_scores, experts):
    tok_rows, top_count = expert_ids.shape
    capacity = tok_rows * top_count * 3 // (2 * experts)
    flat_ids = expert_ids.reshape(-1)
    onehot = (flat_ids[:, None] == jnp.arange(experts, dtype=jnp.int32)[None, :]).astype(jnp.int32)
    before = jnp.cumsum(onehot, axis=0) - onehot
    slot_index = jnp.sum(before * onehot, axis=1).reshape(tok_rows, top_count)
    slot_keys = expert_ids * capacity + slot_index
    columns = jnp.arange(experts * capacity, dtype=jnp.int32)
    matches = slot_keys[:, :, None] == columns[None, None, :]
    selector = jnp.any(matches, axis=1).astype(jnp.bfloat16)
    weights = jnp.sum(
        jnp.where(matches, gate_scores[:, :, None].astype(jnp.float32), 0.0), axis=1
    ).astype(jnp.bfloat16)
    return capacity, selector, weights


def transposed_down(w):
    groups = lax.axis_size("group")
    me = lax.axis_index("group")
    width = w.shape[1] // groups
    received = [lax.dynamic_slice_in_dim(w, me * width, width, axis=1)]
    for s in range(1, groups):
        dest = (me + groups - s) % groups
        piece = lax.dynamic_slice_in_dim(w, dest * width, width, axis=1)
        received.append(
            lax.ppermute(piece, "group", [(j, (j - s) % groups) for j in range(groups)])
        )
    stacked = jnp.stack(received)
    return jnp.roll(stacked, me, axis=0).reshape(groups * w.shape[0], width)


def layer(tokens, gate_weight, up_weight, down_weight, expert_ids, gate_scores):
    experts = lax.axis_size("expert")
    capacity, selector, weights = route_tables(expert_ids, gate_scores, experts)
    placed = lax.dot_general(
        selector, tokens, (((0,), (0,)), ((), ())), preferred_element_type=jnp.float32
    ).astype(jnp.bfloat16)
    down_cols = transposed_down(down_weight[0])
    arrived = lax.all_to_all(
        placed.reshape(experts, capacity, tokens.shape[1]), "expert", 0, 0, tiled=True
    ).reshape(experts * capacity, tokens.shape[1])
    row_block = lax.all_gather(arrived, "group", axis=1, tiled=True)

    gate_value = lax.dot_general(
        row_block, gate_weight[0], (((1,), (1,)), ((), ())), preferred_element_type=jnp.float32
    )
    up_value = lax.dot_general(
        row_block, up_weight[0], (((1,), (1,)), ((), ())), preferred_element_type=jnp.float32
    )
    hidden = (jax.nn.silu(gate_value) * up_value).astype(jnp.bfloat16)
    hidden_all = lax.all_gather(hidden, "group", axis=1, tiled=True)
    partial_value = jnp.dot(hidden_all, down_cols, preferred_element_type=jnp.float32)
    returned = lax.all_to_all(
        partial_value.astype(jnp.bfloat16).reshape(experts, capacity, -1), "expert", 0, 0, tiled=True
    ).reshape(experts * capacity, -1)
    combined = jnp.dot(weights, returned, preferred_element_type=jnp.float32)
    return combined.astype(jnp.bfloat16)


def solution(mesh):
    placed = (
        P("expert", "group"),
        P("expert", "group", None),
        P("expert", "group", None),
        P("expert", "group", None),
        P("expert", None),
        P("expert", None),
    )
    return jax.shard_map(
        layer, mesh=mesh, in_specs=placed, out_specs=P("expert", "group"), check_vma=False
    )
```

```python
import jax
import jax.numpy as jnp
from jax import lax
from jax.sharding import PartitionSpec as P


def route_tables(expert_ids, gate_scores, experts):
    tok_rows, top_count = expert_ids.shape
    capacity = tok_rows * top_count * 3 // (2 * experts)
    flat_ids = expert_ids.reshape(-1)
    onehot = (flat_ids[:, None] == jnp.arange(experts, dtype=jnp.int32)[None, :]).astype(jnp.int32)
    before = jnp.cumsum(onehot, axis=0) - onehot
    slot_index = jnp.sum(before * onehot, axis=1).reshape(tok_rows, top_count)
    slot_keys = expert_ids * capacity + slot_index
    columns = jnp.arange(experts * capacity, dtype=jnp.int32)
    matches = slot_keys[:, :, None] == columns[None, None, :]
    selector = jnp.any(matches, axis=1).astype(jnp.bfloat16)
    weights = jnp.sum(
        jnp.where(matches, gate_scores[:, :, None].astype(jnp.float32), 0.0), axis=1
    ).astype(jnp.bfloat16)
    return capacity, selector, weights


def transposed_down(w):
    groups = lax.axis_size("group")
    me = lax.axis_index("group")
    width = w.shape[1] // groups
    by_dest = jnp.roll(w.reshape(w.shape[0], groups, width), -me, axis=1)
    received = [by_dest[:, 0]]
    for s in range(1, groups):
        piece = by_dest[:, groups - s]
        received.append(
            lax.ppermute(piece, "group", [(j, (j - s) % groups) for j in range(groups)])
        )
    return jnp.concatenate(received, axis=0)


def layer(tokens, gate_weight, up_weight, down_weight, expert_ids, gate_scores):
    experts = lax.axis_size("expert")
    capacity, selector, weights = route_tables(expert_ids, gate_scores, experts)
    placed = lax.dot_general(
        selector, tokens, (((0,), (0,)), ((), ())), preferred_element_type=jnp.float32
    ).astype(jnp.bfloat16)
    down_cols = transposed_down(down_weight[0])
    arrived = lax.all_to_all(
        placed.reshape(experts, capacity, tokens.shape[1]), "expert", 0, 0, tiled=True
    ).reshape(experts * capacity, tokens.shape[1])
    row_block = lax.all_gather(arrived, "group", axis=1, tiled=True)

    gate_value = lax.dot_general(
        row_block, gate_weight[0], (((1,), (1,)), ((), ())), preferred_element_type=jnp.float32
    )
    up_value = lax.dot_general(
        row_block, up_weight[0], (((1,), (1,)), ((), ())), preferred_element_type=jnp.float32
    )
    hidden = (jax.nn.silu(gate_value) * up_value).astype(jnp.bfloat16)
    hidden_all = lax.all_gather(hidden, "group", axis=1, tiled=True)
    groups = lax.axis_size("group")
    hidden_all = jnp.roll(
        hidden_all.reshape(hidden.shape[0], groups, hidden.shape[1]), -lax.axis_index("group"), axis=1
    ).reshape(hidden.shape[0], -1)
    partial_value = jnp.dot(hidden_all, down_cols, preferred_element_type=jnp.float32)
    returned = lax.all_to_all(
        partial_value.astype(jnp.bfloat16).reshape(experts, capacity, -1), "expert", 0, 0, tiled=True
    ).reshape(experts * capacity, -1)
    combined = jnp.dot(weights, returned, preferred_element_type=jnp.float32)
    return combined.astype(jnp.bfloat16)


def solution(mesh):
    placed = (
        P("expert", "group"),
        P("expert", "group", None),
        P("expert", "group", None),
        P("expert", "group", None),
        P("expert", None),
        P("expert", None),
    )
    return jax.shard_map(layer, mesh=mesh, in_specs=placed, out_specs=P("expert", "group"), check_vma=False)
```

```python
import jax
import jax.numpy as jnp
from jax import lax
from jax.sharding import PartitionSpec as P


def route_tables(expert_ids, gate_scores, experts):
    tok_rows, top_count = expert_ids.shape
    capacity = tok_rows * top_count * 3 // (2 * experts)
    flat_ids = expert_ids.reshape(-1)
    onehot = (flat_ids[:, None] == jnp.arange(experts, dtype=jnp.int32)[None, :]).astype(jnp.int32)
    before = jnp.cumsum(onehot, axis=0) - onehot
    slot_index = jnp.sum(before * onehot, axis=1).reshape(tok_rows, top_count)
    slot_keys = expert_ids * capacity + slot_index
    columns = jnp.arange(experts * capacity, dtype=jnp.int32)
    matches = slot_keys[:, :, None] == columns[None, None, :]
    selector = jnp.any(matches, axis=1).astype(jnp.bfloat16)
    weights = jnp.sum(
        jnp.where(matches, gate_scores[:, :, None].astype(jnp.float32), 0.0), axis=1
    ).astype(jnp.bfloat16)
    return capacity, selector, weights


def per_device(tokens, gate_weight, up_weight, down_weight, expert_ids, gate_scores):
    experts = lax.axis_size("expert")
    capacity, selector, weights = route_tables(expert_ids, gate_scores, experts)
    placed = lax.dot_general(
        selector, tokens, (((0,), (0,)), ((), ())), preferred_element_type=jnp.float32
    ).astype(jnp.bfloat16)
    arrived = lax.all_to_all(
        placed.reshape(experts, capacity, tokens.shape[1]), "expert", 0, 0, tiled=True
    ).reshape(experts * capacity, tokens.shape[1])
    row_block = lax.all_gather(arrived, "group", axis=1, tiled=True)
    gate_value = lax.dot_general(
        row_block, gate_weight[0], (((1,), (1,)), ((), ())), preferred_element_type=jnp.float32
    )
    up_value = lax.dot_general(
        row_block, up_weight[0], (((1,), (1,)), ((), ())), preferred_element_type=jnp.float32
    )
    hidden = (jax.nn.silu(gate_value) * up_value).astype(jnp.bfloat16)
    hidden_all = lax.all_gather(hidden, "group", axis=1, tiled=True)
    down_cols = lax.all_to_all(down_weight[0], "group", 1, 0, tiled=True)
    partial_value = jnp.dot(hidden_all, down_cols, preferred_element_type=jnp.float32)
    returned = lax.all_to_all(
        partial_value.astype(jnp.bfloat16).reshape(experts, capacity, -1), "expert", 0, 0, tiled=True
    ).reshape(experts * capacity, -1)
    combined = jnp.dot(weights, returned, preferred_element_type=jnp.float32)
    return combined.astype(jnp.bfloat16)


def solution(mesh):
    placed = (
        P("expert", "group"),
        P("expert", "group", None),
        P("expert", "group", None),
        P("expert", "group", None),
        P("expert", None),
        P("expert", None),
    )
    return jax.shard_map(
        per_device, mesh=mesh, in_specs=placed, out_specs=P("expert", "group"), check_vma=False
    )
```

```python
import jax
import jax.numpy as jnp
from jax import lax
from jax.sharding import PartitionSpec as P


def route_tables(expert_ids, gate_scores, experts):
    tok_rows, top_count = expert_ids.shape
    capacity = tok_rows * top_count * 3 // (2 * experts)
    flat_ids = expert_ids.reshape(-1)
    onehot = (flat_ids[:, None] == jnp.arange(experts, dtype=jnp.int32)[None, :]).astype(jnp.int32)
    before = jnp.cumsum(onehot, axis=0) - onehot
    slot_index = jnp.sum(before * onehot, axis=1).reshape(tok_rows, top_count)
    slot_keys = expert_ids * capacity + slot_index
    columns = jnp.arange(experts * capacity, dtype=jnp.int32)
    matches = slot_keys[:, :, None] == columns[None, None, :]
    selector = jnp.any(matches, axis=1).astype(jnp.bfloat16)
    weights = jnp.sum(
        jnp.where(matches, gate_scores[:, :, None].astype(jnp.float32), 0.0), axis=1
    ).astype(jnp.bfloat16)
    return capacity, selector, weights


def layer(tokens, gate_weight, up_weight, down_weight, expert_ids, gate_scores):
    experts = lax.axis_size("expert")
    capacity, selector, weights = route_tables(expert_ids, gate_scores, experts)
    placed = lax.dot_general(
        selector, tokens, (((0,), (0,)), ((), ())), preferred_element_type=jnp.float32
    ).astype(jnp.bfloat16)
    arrived = lax.all_to_all(
        placed.reshape(experts, capacity, tokens.shape[1]), "expert", 0, 0, tiled=True
    ).reshape(experts * capacity, tokens.shape[1])
    row_block = lax.all_gather(arrived, "group", axis=1, tiled=True)
    down_cols = lax.all_to_all(down_weight[0], "group", 1, 0, tiled=True)
    gate_value = lax.dot_general(
        row_block, gate_weight[0], (((1,), (1,)), ((), ())), preferred_element_type=jnp.float32
    )
    up_value = lax.dot_general(
        row_block, up_weight[0], (((1,), (1,)), ((), ())), preferred_element_type=jnp.float32
    )
    hidden = (jax.nn.silu(gate_value) * up_value).astype(jnp.bfloat16)
    slots = hidden.reshape(experts, capacity, hidden.shape[1])
    cut = capacity // 2
    pieces = []
    for c in range(2):
        part = slots[:, c * cut:(c + 1) * cut].reshape(experts * cut, hidden.shape[1])
        hidden_all = lax.all_gather(part, "group", axis=1, tiled=True)
        partial_value = jnp.dot(hidden_all, down_cols, preferred_element_type=jnp.float32)
        pieces.append(
            lax.all_to_all(
                partial_value.astype(jnp.bfloat16).reshape(experts, cut, -1), "expert", 0, 0, tiled=True
            )
        )
    returned = jnp.concatenate(pieces, axis=1).reshape(experts * capacity, -1)
    combined = jnp.dot(weights, returned, preferred_element_type=jnp.float32)
    return combined.astype(jnp.bfloat16)


def solution(mesh):
    placed = (
        P("expert", "group"),
        P("expert", "group", None),
        P("expert", "group", None),
        P("expert", "group", None),
        P("expert", None),
        P("expert", None),
    )
    return jax.shard_map(
        layer, mesh=mesh, in_specs=placed, out_specs=P("expert", "group"), check_vma=False
    )
```

```python
import jax
import jax.numpy as jnp
from jax import lax
from jax.sharding import PartitionSpec as P


def route_tables(expert_ids, gate_scores, experts):
    tok_rows, top_count = expert_ids.shape
    capacity = tok_rows * top_count * 3 // (2 * experts)
    flat_ids = expert_ids.reshape(-1)
    onehot = (flat_ids[:, None] == jnp.arange(experts, dtype=jnp.int32)[None, :]).astype(jnp.int32)
    before = jnp.cumsum(onehot, axis=0) - onehot
    slot_index = jnp.sum(before * onehot, axis=1).reshape(tok_rows, top_count)
    slot_keys = expert_ids * capacity + slot_index
    columns = jnp.arange(experts * capacity, dtype=jnp.int32)
    matches = slot_keys[:, :, None] == columns[None, None, :]
    selector = jnp.any(matches, axis=1).astype(jnp.bfloat16)
    weights = jnp.sum(
        jnp.where(matches, gate_scores[:, :, None].astype(jnp.float32), 0.0), axis=1
    ).astype(jnp.bfloat16)
    return capacity, selector, weights


def layer(tokens, gate_weight, up_weight, down_weight, expert_ids, gate_scores):
    experts = lax.axis_size("expert")
    capacity, selector, weights = route_tables(expert_ids, gate_scores, experts)
    placed = lax.dot_general(
        selector, tokens, (((0,), (0,)), ((), ())), preferred_element_type=jnp.float32
    ).astype(jnp.bfloat16)
    arrived = lax.all_to_all(
        placed.reshape(experts, capacity * tokens.shape[1]), "expert", 0, 0, tiled=True
    ).reshape(experts * capacity, tokens.shape[1])
    row_block = lax.all_gather(arrived, "group", axis=1, tiled=True)
    down_cols = lax.all_to_all(down_weight[0], "group", 1, 0, tiled=True)
    gate_value = lax.dot_general(
        row_block, gate_weight[0], (((1,), (1,)), ((), ())), preferred_element_type=jnp.float32
    )
    up_value = lax.dot_general(
        row_block, up_weight[0], (((1,), (1,)), ((), ())), preferred_element_type=jnp.float32
    )
    hidden = (jax.nn.silu(gate_value) * up_value).astype(jnp.bfloat16)
    hidden_all = lax.all_gather(hidden, "group", axis=1, tiled=True)
    partial_value = jnp.dot(hidden_all, down_cols, preferred_element_type=jnp.float32)
    returned = lax.all_to_all(
        partial_value.astype(jnp.bfloat16).reshape(experts, -1), "expert", 0, 0, tiled=True
    ).reshape(experts * capacity, -1)
    combined = jnp.dot(weights, returned, preferred_element_type=jnp.float32)
    return combined.astype(jnp.bfloat16)


def solution(mesh):
    placed = (
        P("expert", "group"),
        P("expert", "group", None),
        P("expert", "group", None),
        P("expert", "group", None),
        P("expert", None),
        P("expert", None),
    )
    return jax.shard_map(
        layer, mesh=mesh, in_specs=placed, out_specs=P("expert", "group"), check_vma=False
    )
```
